128 devices in a mesh: expert: 64 (over x, z, y_hi, core), dp: 2 (over y_lo).
Axes of the slice: x: 4, y: 4 (y_hi: 2, y_lo: 2; y = y_hi * 2 + y_lo), z: 4, core: 2. Of those that a mesh axis runs over, the one named last changes fastest.
Arguments:
- tokens: bfloat16 [16384, 3584], P(('expert', 'dp')), may hold values from -6 to 6
- cotangent: bfloat16 [16384, 1024], P(('expert', 'dp')), may hold values from -4 to 4
- routing: int32 [16384, 1], P(('expert', 'dp')), may hold values from 0 to 63, as said below
- w_gate: bfloat16 [64, 3584, 1024], P('expert', None, 'dp'), may hold values from -0.09375 to 0.09375
- w_up: bfloat16 [64, 3584, 1024], P('expert', None, 'dp'), may hold values from -0.09375 to 0.09375
Outputs:
- grad_tokens: bfloat16 [16384, 3584], P(('expert', 'dp'))
- grad_gate: bfloat16 [64, 3584, 1024], P('expert', None, 'dp')
- grad_up: bfloat16 [64, 3584, 1024], P('expert', None, 'dp')
The draws below stay inside these ranges and needn't reach their ends.
Inputs may be any that keep to these rules, and one draw needn't show every extreme that they name: `routing`: among the rows of one device no expert is named more than 4 times, and some device names some expert exactly 4 times. Of the experts e and e + 32, one is drawn busy and the other quiet.
All inputs are finite; a program needn't handle non-finite values.
Results may differ from the reference program's by a relative error of at most 0.005.
Values may be sent and summed in bfloat16 or wider, within the bound.
No kernel may reach another device: no remote copies, remote signals or barrier semaphores. Data moves between devices by JAX's collectives and lax.ppermute only.
A program may use at most 128 MiB of HBM per device.

```python
import jax
import jax.numpy as jnp
from jax import lax

D = 3584
FF = 1024
TOK_DEV = 128
TOKENS = 16384
EXPERTS = 64
MOST = 4
N_EXPERT = 64
N_DP = 2


def draw_routing(key, part):
    block_count = TOKENS // TOK_DEV
    slot_count = EXPERTS * MOST
    half_count = EXPERTS // 2
    key_side, key_factor, key_score, key_full, key_order = jax.random.split(key, 5)
    busy_side = jax.random.randint(key_side, (half_count,), 0, 2).astype(jnp.int32)
    busy_factor = jax.random.randint(key_factor, (half_count,), 2, 7).astype(jnp.int32)
    expert_ids = jnp.arange(EXPERTS, dtype=jnp.int32)
    pair_of = expert_ids % half_count
    is_busy = expert_ids // half_count == busy_side[pair_of]
    weight_of = jnp.where(is_busy, busy_factor[pair_of], 1).astype(jnp.int32)
    slot_expert = (jnp.arange(slot_count, dtype=jnp.int32) // MOST).astype(jnp.int32)
    raw_score = jax.random.randint(key_score, (block_count, slot_count), 0, 4096).astype(jnp.int32)
    score = raw_score * weight_of[slot_expert][None, :]
    full_expert = jax.random.randint(key_full, (block_count,), 0, EXPERTS).astype(jnp.int32)
    score = score + jnp.where(slot_expert[None, :] == full_expert[:, None], 65536, 0).astype(jnp.int32)
    distinct = score * slot_count + jnp.arange(slot_count, dtype=jnp.int32)[None, :]
    top_values, top_index = lax.top_k(distinct, TOK_DEV)
    chosen = (top_index.astype(jnp.int32) // MOST).astype(jnp.int32)
    order_score = jax.random.randint(key_order, (block_count, TOK_DEV), 0, 65536).astype(jnp.int32) * TOK_DEV + jnp.arange(TOK_DEV, dtype=jnp.int32)[None, :]
    order = jnp.argsort(order_score, axis=1).astype(jnp.int32)
    chosen = jnp.take_along_axis(chosen, order, axis=1)
    return chosen.reshape(TOKENS, 1).astype(jnp.int32)


def block_levels(own_key, shape, pieces, low, high):
    level, own = 1.0, jax.random.fold_in(own_key, 6)
    for position, blocks in pieces:
        steps = jnp.exp(jax.random.uniform(jax.random.fold_in(own, position), (blocks,), jnp.float32, low / len(pieces), high / len(pieces)))
        level = level * jnp.repeat(steps, shape[position] // blocks).reshape([-1 if axis == position else 1 for axis in range(len(shape))])
    return level


def centred(key, shape, scale, limit, pieces=(), kind=jnp.bfloat16):
    array = scale * jax.random.normal(key, shape, jnp.float32)
    if pieces:
        array = array * block_levels(key, shape, pieces, -0.22, 0.18)
    return jnp.clip(array, -limit, limit).astype(kind)


def setup_inputs(seed: int = 0) -> dict:
    key_list = jax.random.split(jax.random.key(seed), 6)
    tokens = centred(key_list[0], (TOKENS, D), 1.0, 6.0, ((0, 128),))
    cotangent = centred(key_list[1], (TOKENS, FF), 0.5, 4.0, ((0, 128),))
    routing = draw_routing(jax.random.fold_in(key_list[5], 71), 0)
    w_gate = centred(key_list[3], (EXPERTS, D, FF), D ** -0.5, 0.09375, ((0, 64), (2, 2)))
    w_up = centred(key_list[4], (EXPERTS, D, FF), D ** -0.5, 0.09375, ((0, 64), (2, 2)))
    return {"tokens": tokens, "cotangent": cotangent, "routing": routing, "w_gate": w_gate, "w_up": w_up}


def reference(tokens, cotangent, routing, w_gate, w_up):
    expert_of = routing[:, 0].astype(jnp.int32)
    token_total = tokens.shape[0]
    model_width = tokens.shape[1]
    sort_order = jnp.argsort(expert_of, stable=True).astype(jnp.int32)
    expert_counts = jnp.sum((expert_of[:, None] == jnp.arange(EXPERTS, dtype=jnp.int32)[None, :]).astype(jnp.int32), axis=0).astype(jnp.int32)
    expert_starts = (jnp.cumsum(expert_counts) - expert_counts).astype(jnp.int32)
    capacity = N_EXPERT * N_DP * MOST
    slot_range = jnp.arange(capacity, dtype=jnp.int32)
    padded_tokens = jnp.concatenate([tokens, jnp.zeros((1, model_width), tokens.dtype)], axis=0)
    padded_cotangent = jnp.concatenate([cotangent, jnp.zeros((1, cotangent.shape[1]), cotangent.dtype)], axis=0)

    def per_expert(expert):
        picked = jnp.clip(expert_starts[expert] + slot_range, 0, token_total - 1).astype(jnp.int32)
        row_index = jnp.where(slot_range < expert_counts[expert], sort_order[picked], token_total).astype(jnp.int32)
        row_block = padded_tokens[row_index]
        cot_block = padded_cotangent[row_index]
        weight_gate = w_gate[expert]
        weight_up = w_up[expert]
        gate_act = jnp.dot(row_block, weight_gate, preferred_element_type=jnp.float32)
        up_act = jnp.dot(row_block, weight_up, preferred_element_type=jnp.float32)
        sigmoid_gate = jax.nn.sigmoid(gate_act)
        cot_float = cot_block.astype(jnp.float32)
        d_up = (cot_float * gate_act * sigmoid_gate).astype(jnp.bfloat16)
        d_gate = (cot_float * up_act * sigmoid_gate * (1.0 + gate_act * (1.0 - sigmoid_gate))).astype(jnp.bfloat16)
        back_rows = jnp.dot(d_gate, weight_gate.T, preferred_element_type=jnp.float32) + jnp.dot(d_up, weight_up.T, preferred_element_type=jnp.float32)
        grad_g = jnp.dot(row_block.T, d_gate, preferred_element_type=jnp.float32)
        grad_u = jnp.dot(row_block.T, d_up, preferred_element_type=jnp.float32)
        return back_rows.astype(jnp.bfloat16), grad_g.astype(jnp.bfloat16), grad_u.astype(jnp.bfloat16), row_index

    back_all, grad_gate, grad_up, index_all = lax.map(per_expert, jnp.arange(EXPERTS, dtype=jnp.int32))
    grad_tokens = jnp.zeros((token_total + 1, model_width), jnp.bfloat16).at[index_all.reshape(-1)].set(back_all.reshape(-1, model_width))
    return grad_tokens[:token_total], grad_gate, grad_up
```

```python
import jax
import jax.numpy as jnp
from jax import lax
from jax.sharding import PartitionSpec as P


def expert_math(rows, cot, weight_gate, weight_up):
    gate_act = jnp.dot(rows, weight_gate, preferred_element_type=jnp.float32)
    up_act = jnp.dot(rows, weight_up, preferred_element_type=jnp.float32)
    sigmoid_gate = jax.nn.sigmoid(gate_act)
    cot_float = cot.astype(jnp.float32)
    d_up = (cot_float * gate_act * sigmoid_gate).astype(jnp.bfloat16)
    d_gate = (
        cot_float * up_act * sigmoid_gate * (1.0 + gate_act * (1.0 - sigmoid_gate))
    ).astype(jnp.bfloat16)
    back = lax.dot_general(
        d_gate, weight_gate, (((1,), (1,)), ((), ())), preferred_element_type=jnp.float32
    )
    back = back + lax.dot_general(
        d_up, weight_up, (((1,), (1,)), ((), ())), preferred_element_type=jnp.float32
    )
    grad_g = lax.dot_general(
        rows, d_gate, (((0,), (0,)), ((), ())), preferred_element_type=jnp.float32
    )
    grad_u = lax.dot_general(
        rows, d_up, (((0,), (0,)), ((), ())), preferred_element_type=jnp.float32
    )
    return back.astype(jnp.bfloat16), grad_g.astype(jnp.bfloat16), grad_u.astype(jnp.bfloat16)


def per_device(tokens, cotangent, routing, w_gate, w_up):
    n_experts = lax.axis_size("expert")
    n_dp = lax.axis_size("dp")
    tok_rows, model_width = tokens.shape
    hidden = cotangent.shape[1]
    half_width = hidden // n_dp
    most_rows = max(2, tok_rows // 32, tok_rows // n_experts)
    slot_total = n_experts * most_rows

    expert_of = routing[:, 0]
    one_hot = (expert_of[:, None] == jnp.arange(n_experts, dtype=jnp.int32)[None, :]).astype(
        jnp.int32
    )
    slot_of = jnp.sum(jnp.cumsum(one_hot, axis=0) * one_hot, axis=1) - 1
    dest = expert_of * most_rows + slot_of
    pick = (jnp.arange(slot_total, dtype=jnp.int32)[:, None] == dest[None, :]).astype(
        jnp.bfloat16
    )
    send_rows = jnp.dot(pick, tokens, preferred_element_type=jnp.float32).astype(jnp.bfloat16)
    send_cot = jnp.dot(pick, cotangent, preferred_element_type=jnp.float32).astype(jnp.bfloat16)
    send_rows = send_rows.reshape(n_experts, 1, most_rows, model_width)
    send_cot = jnp.swapaxes(
        send_cot.reshape(n_experts, most_rows, n_dp, half_width), 1, 2
    )
    packed = jnp.concatenate(
        [
            jnp.broadcast_to(send_rows, (n_experts, n_dp, most_rows, model_width)),
            send_cot,
        ],
        axis=3,
    ).reshape(n_experts * n_dp * most_rows, model_width + half_width)
    got = lax.all_to_all(packed, ("expert", "dp"), split_axis=0, concat_axis=0, tiled=True)
    got_rows = got[:, :model_width]
    got_cot = got[:, model_width:]

    back, grad_g, grad_u = expert_math(got_rows, got_cot, w_gate[0], w_up[0])

    returned = lax.all_to_all(back, ("expert", "dp"), split_axis=0, concat_axis=0, tiled=True)
    returned = returned.reshape(n_experts, n_dp, most_rows, model_width).astype(jnp.float32)
    summed = jnp.sum(returned, axis=1).astype(jnp.bfloat16).reshape(slot_total, model_width)
    grad_tokens = lax.dot_general(
        pick, summed, (((0,), (0,)), ((), ())), preferred_element_type=jnp.float32
    ).astype(jnp.bfloat16)
    return grad_tokens, grad_g[None], grad_u[None]


def solution(mesh):
    placed = (
        P(("expert", "dp"), None),
        P(("expert", "dp"), None),
        P(("expert", "dp"), None),
        P("expert", None, "dp"),
        P("expert", None, "dp"),
    )
    return jax.shard_map(
        per_device,
        mesh=mesh,
        in_specs=placed,
        out_specs=(P(("expert", "dp"), None), P("expert", None, "dp"), P("expert", None, "dp")),
        check_vma=False,
    )
```

```python
import jax
import jax.numpy as jnp
from jax import lax
from jax.sharding import PartitionSpec as P

AXES = ("expert", "dp")


def hidden_grads(rows, cot, weight_gate, weight_up):
    gate_act = jnp.dot(rows, weight_gate, preferred_element_type=jnp.float32)
    up_act = jnp.dot(rows, weight_up, preferred_element_type=jnp.float32)
    sigmoid_gate = jax.nn.sigmoid(gate_act)
    cot_float = cot.astype(jnp.float32)
    d_up = (cot_float * gate_act * sigmoid_gate).astype(jnp.bfloat16)
    d_gate = (
        cot_float * up_act * sigmoid_gate * (1.0 + gate_act * (1.0 - sigmoid_gate))
    ).astype(jnp.bfloat16)
    back = lax.dot_general(
        d_gate, weight_gate, (((1,), (1,)), ((), ())), preferred_element_type=jnp.float32
    )
    back = back + lax.dot_general(
        d_up, weight_up, (((1,), (1,)), ((), ())), preferred_element_type=jnp.float32
    )
    return back.astype(jnp.bfloat16), d_gate, d_up


def per_device(tokens, cotangent, routing, w_gate, w_up):
    n_experts = lax.axis_size("expert")
    n_dp = lax.axis_size("dp")
    tok_rows, model_width = tokens.shape
    hidden = cotangent.shape[1]
    half_width = hidden // n_dp
    most_rows = max(2, tok_rows // 32, tok_rows // n_experts)
    chunk_slots = 2 if most_rows % 2 == 0 else 1
    n_chunks = most_rows // chunk_slots
    wide = model_width + half_width
    weight_gate = w_gate[0]
    weight_up = w_up[0]

    expert_of = routing[:, 0]
    one_hot = (expert_of[:, None] == jnp.arange(n_experts, dtype=jnp.int32)[None, :]).astype(
        jnp.int32
    )
    slot_of = jnp.sum(jnp.cumsum(one_hot, axis=0) * one_hot, axis=1) - 1
    pick = (
        (expert_of[None, None, :] == jnp.arange(n_experts, dtype=jnp.int32)[:, None, None])
        & (slot_of[None, None, :] == jnp.arange(most_rows, dtype=jnp.int32)[None, :, None])
    ).astype(jnp.bfloat16)
    sel_rows = jnp.einsum(
        "est,td->esd", pick, tokens, preferred_element_type=jnp.float32
    ).astype(jnp.bfloat16)
    sel_cot = jnp.einsum(
        "est,tf->esf", pick, cotangent, preferred_element_type=jnp.float32
    ).astype(jnp.bfloat16)
    sel_cot = sel_cot.reshape(n_experts, most_rows, n_dp, half_width)

    got_rows, got_cot = [], []
    for chunk in range(n_chunks):
        slots = slice(chunk * chunk_slots, (chunk + 1) * chunk_slots)
        part_rows = jnp.broadcast_to(
            sel_rows[:, None, slots], (n_experts, n_dp, chunk_slots, model_width)
        )
        part_cot = jnp.swapaxes(sel_cot[:, slots], 1, 2)
        packed = jnp.concatenate([part_rows, part_cot], axis=3).reshape(
            n_experts * n_dp, chunk_slots * wide
        )
        got = lax.all_to_all(packed, AXES, split_axis=0, concat_axis=0, tiled=True)
        for j in range(chunk_slots):
            got_rows.append(got[:, j * wide : j * wide + model_width])
            got_cot.append(got[:, j * wide + model_width : (j + 1) * wide])

    backs, d_gates, d_ups = [], [], []
    for chunk in range(n_chunks):
        parts = []
        for j in range(chunk_slots):
            slot = chunk * chunk_slots + j
            back, d_gate, d_up = hidden_grads(
                got_rows[slot], got_cot[slot], weight_gate, weight_up
            )
            parts.append(back)
            d_gates.append(d_gate)
            d_ups.append(d_up)
        backs.append(
            lax.all_to_all(
                jnp.concatenate(parts, axis=1), AXES, split_axis=0, concat_axis=0, tiled=True
            )
        )

    all_rows = jnp.concatenate(got_rows, axis=0)
    grad_g = lax.dot_general(
        all_rows,
        jnp.concatenate(d_gates, axis=0),
        (((0,), (0,)), ((), ())),
        preferred_element_type=jnp.float32,
    ).astype(jnp.bfloat16)
    grad_u = lax.dot_general(
        all_rows,
        jnp.concatenate(d_ups, axis=0),
        (((0,), (0,)), ((), ())),
        preferred_element_type=jnp.float32,
    ).astype(jnp.bfloat16)

    pick_dup = jnp.broadcast_to(
        pick[:, None], (n_experts, n_dp, most_rows, tok_rows)
    ).reshape(n_experts * n_dp, most_rows, tok_rows)
    total = None
    for chunk in range(n_chunks):
        for j in range(chunk_slots):
            slot = chunk * chunk_slots + j
            part = lax.dot_general(
                pick_dup[:, slot],
                backs[chunk][:, j * model_width : (j + 1) * model_width],
                (((0,), (0,)), ((), ())),
                preferred_element_type=jnp.float32,
            )
            total = part if total is None else total + part
    return total.astype(jnp.bfloat16), grad_g[None], grad_u[None]


def solution(mesh):
    placed = (
        P(AXES, None),
        P(AXES, None),
        P(AXES, None),
        P("expert", None, "dp"),
        P("expert", None, "dp"),
    )
    return jax.shard_map(
        per_device,
        mesh=mesh,
        in_specs=placed,
        out_specs=(P(AXES, None), P("expert", None, "dp"), P("expert", None, "dp")),
        check_vma=False,
    )
```

```python
import jax
import jax.numpy as jnp
from jax import lax
from jax.sharding import PartitionSpec as P


def expert_math(rows, cot, weight_gate, weight_up):
    gate_act = jnp.einsum("skd,df->skf", rows, weight_gate, preferred_element_type=jnp.float32)
    up_act = jnp.einsum("skd,df->skf", rows, weight_up, preferred_element_type=jnp.float32)
    sigmoid_gate = jax.nn.sigmoid(gate_act)
    cot_float = cot.astype(jnp.float32)
    d_up = (cot_float * gate_act * sigmoid_gate).astype(jnp.bfloat16)
    d_gate = (
        cot_float * up_act * sigmoid_gate * (1.0 + gate_act * (1.0 - sigmoid_gate))
    ).astype(jnp.bfloat16)
    back = jnp.einsum("skf,df->skd", d_gate, weight_gate, preferred_element_type=jnp.float32)
    back = back + jnp.einsum("skf,df->skd", d_up, weight_up, preferred_element_type=jnp.float32)
    grad_g = jnp.einsum("skd,skf->df", rows, d_gate, preferred_element_type=jnp.float32)
    grad_u = jnp.einsum("skd,skf->df", rows, d_up, preferred_element_type=jnp.float32)
    return back.astype(jnp.bfloat16), grad_g.astype(jnp.bfloat16), grad_u.astype(jnp.bfloat16)


def per_device(tokens, cotangent, routing, w_gate, w_up):
    n_experts = lax.axis_size("expert")
    n_dp = lax.axis_size("dp")
    tok_rows, model_width = tokens.shape
    hidden = cotangent.shape[1]
    half_width = hidden // n_dp
    most_rows = max(2, tok_rows // 32, tok_rows // n_experts)
    slot_total = n_experts * most_rows

    expert_of = routing[:, 0]
    one_hot = (expert_of[:, None] == jnp.arange(n_experts, dtype=jnp.int32)[None, :]).astype(
        jnp.int32
    )
    slot_of = jnp.sum(jnp.cumsum(one_hot, axis=0) * one_hot, axis=1) - 1
    dest = expert_of * most_rows + slot_of
    pick = (jnp.arange(slot_total, dtype=jnp.int32)[:, None] == dest[None, :]).astype(
        jnp.bfloat16
    )
    send_rows = jnp.dot(pick, tokens, preferred_element_type=jnp.float32).astype(jnp.bfloat16)
    send_cot = jnp.dot(pick, cotangent, preferred_element_type=jnp.float32).astype(jnp.bfloat16)
    send_rows = send_rows.reshape(n_experts, 1, most_rows, model_width)
    send_cot = jnp.swapaxes(
        send_cot.reshape(n_experts, most_rows, n_dp, half_width), 1, 2
    )
    packed = jnp.concatenate(
        [
            jnp.broadcast_to(send_rows, (n_experts, n_dp, most_rows, model_width)),
            send_cot,
        ],
        axis=3,
    ).reshape(n_experts * n_dp * most_rows, model_width + half_width)
    packed = packed.reshape(n_experts * n_dp, most_rows, model_width + half_width)
    got = lax.all_to_all(packed, ("expert", "dp"), split_axis=0, concat_axis=0, tiled=True)
    got_rows = got[:, :, :model_width]
    got_cot = got[:, :, model_width:]

    back, grad_g, grad_u = expert_math(got_rows, got_cot, w_gate[0], w_up[0])

    returned = lax.all_to_all(back, ("expert", "dp"), split_axis=0, concat_axis=0, tiled=True)
    pick_dup = jnp.broadcast_to(
        pick.reshape(n_experts, 1, most_rows, tok_rows), (n_experts, n_dp, most_rows, tok_rows)
    ).reshape(n_experts * n_dp, most_rows, tok_rows)
    grad_tokens = lax.dot_general(
        pick_dup, returned, (((0, 1), (0, 1)), ((), ())), preferred_element_type=jnp.float32
    ).astype(jnp.bfloat16)
    return grad_tokens, grad_g[None], grad_u[None]


def solution(mesh):
    placed = (
        P(("expert", "dp"), None),
        P(("expert", "dp"), None),
        P(("expert", "dp"), None),
        P("expert", None, "dp"),
        P("expert", None, "dp"),
    )
    return jax.shard_map(
        per_device,
        mesh=mesh,
        in_specs=placed,
        out_specs=(P(("expert", "dp"), None), P("expert", None, "dp"), P("expert", None, "dp")),
        check_vma=False,
    )
```

```python
import jax
import jax.numpy as jnp
from jax import lax
from jax.sharding import PartitionSpec as P


def expert_math(rows, cot, weight_gate, weight_up):
    gate_act = jnp.einsum("skd,df->skf", rows, weight_gate, preferred_element_type=jnp.float32)
    up_act = jnp.einsum("skd,df->skf", rows, weight_up, preferred_element_type=jnp.float32)
    sigmoid_gate = jax.nn.sigmoid(gate_act)
    cot_float = cot.astype(jnp.float32)
    d_up = (cot_float * gate_act * sigmoid_gate).astype(jnp.bfloat16)
    d_gate = (
        cot_float * up_act * sigmoid_gate * (1.0 + gate_act * (1.0 - sigmoid_gate))
    ).astype(jnp.bfloat16)
    back = jnp.einsum(
        "skf,df->skd",
        jnp.concatenate([d_gate, d_up], axis=2),
        jnp.concatenate([weight_gate, weight_up], axis=1),
        preferred_element_type=jnp.float32,
    )
    grad_g = jnp.einsum("skd,skf->df", rows, d_gate, preferred_element_type=jnp.float32)
    grad_u = jnp.einsum("skd,skf->df", rows, d_up, preferred_element_type=jnp.float32)
    return back.astype(jnp.bfloat16), grad_g.astype(jnp.bfloat16), grad_u.astype(jnp.bfloat16)


def per_device(tokens, cotangent, routing, w_gate, w_up):
    n_experts = lax.axis_size("expert")
    n_dp = lax.axis_size("dp")
    tok_rows, model_width = tokens.shape
    hidden = cotangent.shape[1]
    half_width = hidden // n_dp
    most_rows = max(2, tok_rows // 32, tok_rows // n_experts)
    slot_total = n_experts * most_rows

    expert_of = routing[:, 0]
    one_hot = (expert_of[:, None] == jnp.arange(n_experts, dtype=jnp.int32)[None, :]).astype(
        jnp.int32
    )
    slot_of = jnp.sum(jnp.cumsum(one_hot, axis=0) * one_hot, axis=1) - 1
    dest = expert_of * most_rows + slot_of
    pick = (jnp.arange(slot_total, dtype=jnp.int32)[:, None] == dest[None, :]).astype(
        jnp.bfloat16
    )
    send_rows = jnp.dot(pick, tokens, preferred_element_type=jnp.float32).astype(jnp.bfloat16)
    send_cot = jnp.dot(pick, cotangent, preferred_element_type=jnp.float32).astype(jnp.bfloat16)
    send_rows = send_rows.reshape(n_experts, 1, most_rows, model_width)
    send_cot = jnp.swapaxes(
        send_cot.reshape(n_experts, most_rows, n_dp, half_width), 1, 2
    )
    packed = jnp.concatenate(
        [
            jnp.broadcast_to(send_rows, (n_experts, n_dp, most_rows, model_width)),
            send_cot,
        ],
        axis=3,
    ).reshape(n_experts * n_dp * most_rows, model_width + half_width)
    packed = packed.reshape(n_experts * n_dp, most_rows, model_width + half_width)
    got = lax.all_to_all(packed, ("expert", "dp"), split_axis=0, concat_axis=0, tiled=True)
    got_rows = got[:, :, :model_width]
    got_cot = got[:, :, model_width:]

    back, grad_g, grad_u = expert_math(got_rows, got_cot, w_gate[0], w_up[0])

    returned = lax.all_to_all(back, ("expert", "dp"), split_axis=0, concat_axis=0, tiled=True)
    pick_dup = jnp.broadcast_to(
        pick.reshape(n_experts, 1, most_rows, tok_rows), (n_experts, n_dp, most_rows, tok_rows)
    ).reshape(n_experts * n_dp, most_rows, tok_rows)
    grad_tokens = lax.dot_general(
        pick_dup, returned, (((0, 1), (0, 1)), ((), ())), preferred_element_type=jnp.float32
    ).astype(jnp.bfloat16)
    return grad_tokens, grad_g[None], grad_u[None]


def solution(mesh):
    placed = (
        P(("expert", "dp"), None),
        P(("expert", "dp"), None),
        P(("expert", "dp"), None),
        P("expert", None, "dp"),
        P("expert", None, "dp"),
    )
    return jax.shard_map(
        per_device,
        mesh=mesh,
        in_specs=placed,
        out_specs=(P(("expert", "dp"), None), P("expert", None, "dp"), P("expert", None, "dp")),
        check_vma=False,
    )
```

```python
import jax
import jax.numpy as jnp
from jax import lax
from jax.sharding import PartitionSpec as P


def expert_math(rows, cot, weight_gate, weight_up):
    gate_act = jnp.einsum("skd,df->skf", rows, weight_gate, preferred_element_type=jnp.float32)
    up_act = jnp.einsum("skd,df->skf", rows, weight_up, preferred_element_type=jnp.float32)
    sigmoid_gate = jax.nn.sigmoid(gate_act)
    cot_float = cot.astype(jnp.float32)
    d_up = (cot_float * gate_act * sigmoid_gate).astype(jnp.bfloat16)
    d_gate = (
        cot_float * up_act * sigmoid_gate * (1.0 + gate_act * (1.0 - sigmoid_gate))
    ).astype(jnp.bfloat16)
    back = jnp.einsum(
        "skf,df->skd",
        jnp.concatenate([d_gate, d_up], axis=2),
        jnp.concatenate([weight_gate, weight_up], axis=1),
        preferred_element_type=jnp.float32,
    )
    grad_g = jnp.einsum("skd,skf->df", rows, d_gate, preferred_element_type=jnp.float32)
    grad_u = jnp.einsum("skd,skf->df", rows, d_up, preferred_element_type=jnp.float32)
    return back.astype(jnp.bfloat16), grad_g.astype(jnp.bfloat16), grad_u.astype(jnp.bfloat16)


def per_device(tokens, cotangent, routing, w_gate, w_up):
    n_experts = lax.axis_size("expert")
    n_dp = lax.axis_size("dp")
    tok_rows, model_width = tokens.shape
    hidden = cotangent.shape[1]
    half_width = hidden // n_dp
    most_rows = max(2, tok_rows // 32, tok_rows // n_experts)
    slot_total = n_experts * most_rows

    expert_of = routing[:, 0]
    one_hot = (expert_of[:, None] == jnp.arange(n_experts, dtype=jnp.int32)[None, :]).astype(
        jnp.int32
    )
    slot_of = jnp.sum(jnp.cumsum(one_hot, axis=0) * one_hot, axis=1) - 1
    dest = expert_of * most_rows + slot_of
    pick = (jnp.arange(slot_total, dtype=jnp.int32)[:, None] == dest[None, :]).astype(
        jnp.bfloat16
    )
    stacked = jnp.concatenate(
        [
            jnp.broadcast_to(tokens[None], (n_dp, tok_rows, model_width)),
            jnp.swapaxes(cotangent.reshape(tok_rows, n_dp, half_width), 0, 1),
        ],
        axis=2,
    ).reshape(n_dp * tok_rows, model_width + half_width)
    pick_copy = (
        pick.reshape(n_experts, 1, most_rows, 1, tok_rows)
        * jnp.eye(n_dp, dtype=jnp.bfloat16).reshape(1, n_dp, 1, n_dp, 1)
    ).reshape(n_experts * n_dp * most_rows, n_dp * tok_rows)
    packed = jnp.dot(pick_copy, stacked, preferred_element_type=jnp.float32).astype(jnp.bfloat16)
    packed = packed.reshape(n_experts * n_dp, most_rows, model_width + half_width)
    got = lax.all_to_all(packed, ("expert", "dp"), split_axis=0, concat_axis=0, tiled=True)
    got_rows = got[:, :, :model_width]
    got_cot = got[:, :, model_width:]

    back, grad_g, grad_u = expert_math(got_rows, got_cot, w_gate[0], w_up[0])

    returned = lax.all_to_all(back, ("expert", "dp"), split_axis=0, concat_axis=0, tiled=True)
    pick_dup = jnp.broadcast_to(
        pick.reshape(n_experts, 1, most_rows, tok_rows), (n_experts, n_dp, most_rows, tok_rows)
    ).reshape(n_experts * n_dp, most_rows, tok_rows)
    grad_tokens = lax.dot_general(
        pick_dup, returned, (((0, 1), (0, 1)), ((), ())), preferred_element_type=jnp.float32
    ).astype(jnp.bfloat16)
    return grad_tokens, grad_g[None], grad_u[None]


def solution(mesh):
    placed = (
        P(("expert", "dp"), None),
        P(("expert", "dp"), None),
        P(("expert", "dp"), None),
        P("expert", None, "dp"),
        P("expert", None, "dp"),
    )
    return jax.shard_map(
        per_device,
        mesh=mesh,
        in_specs=placed,
        out_specs=(P(("expert", "dp"), None), P("expert", None, "dp"), P("expert", None, "dp")),
        check_vma=False,
    )
```

```python
import jax
import jax.numpy as jnp
from jax import lax
from jax.sharding import PartitionSpec as P


def expert_math(rows, cot, weight_gate, weight_up):
    gate_act = jnp.einsum("skd,df->skf", rows, weight_gate, preferred_element_type=jnp.float32)
    up_act = jnp.einsum("skd,df->skf", rows, weight_up, preferred_element_type=jnp.float32)
    sigmoid_gate = jax.nn.sigmoid(gate_act)
    cot_float = cot.astype(jnp.float32)
    d_up = (cot_float * gate_act * sigmoid_gate).astype(jnp.bfloat16)
    d_gate = (
        cot_float * up_act * sigmoid_gate * (1.0 + gate_act * (1.0 - sigmoid_gate))
    ).astype(jnp.bfloat16)
    back = jnp.einsum(
        "skf,df->skd",
        jnp.concatenate([d_gate, d_up], axis=2),
        jnp.concatenate([weight_gate, weight_up], axis=1),
        preferred_element_type=jnp.float32,
    )
    grad_g = jnp.einsum("skd,skf->df", rows, d_gate, preferred_element_type=jnp.float32)
    grad_u = jnp.einsum("skd,skf->df", rows, d_up, preferred_element_type=jnp.float32)
    return back, grad_g.astype(jnp.bfloat16), grad_u.astype(jnp.bfloat16)


def per_device(tokens, cotangent, routing, w_gate, w_up):
    n_experts = lax.axis_size("expert")
    n_dp = lax.axis_size("dp")
    tok_rows, model_width = tokens.shape
    hidden = cotangent.shape[1]
    half_width = hidden // n_dp
    most_rows = max(2, tok_rows // 32, tok_rows // n_experts)
    slot_total = n_experts * most_rows

    expert_of = routing[:, 0]
    one_hot = (expert_of[:, None] == jnp.arange(n_experts, dtype=jnp.int32)[None, :]).astype(
        jnp.int32
    )
    slot_of = jnp.sum(jnp.cumsum(one_hot, axis=0) * one_hot, axis=1) - 1
    dest = expert_of * most_rows + slot_of
    pick = (jnp.arange(slot_total, dtype=jnp.int32)[:, None] == dest[None, :]).astype(
        jnp.bfloat16
    )
    send_rows = jnp.dot(pick, tokens, preferred_element_type=jnp.float32).astype(jnp.bfloat16)
    send_cot = jnp.dot(pick, cotangent, preferred_element_type=jnp.float32).astype(jnp.bfloat16)
    send_rows = send_rows.reshape(n_experts, 1, most_rows, model_width)
    send_cot = jnp.swapaxes(
        send_cot.reshape(n_experts, most_rows, n_dp, half_width), 1, 2
    )
    packed = jnp.concatenate(
        [
            jnp.broadcast_to(send_rows, (n_experts, n_dp, most_rows, model_width)),
            send_cot,
        ],
        axis=3,
    ).reshape(n_experts * n_dp * most_rows, model_width + half_width)
    packed = packed.reshape(n_experts * n_dp, most_rows, model_width + half_width)
    got = lax.all_to_all(packed, ("expert", "dp"), split_axis=0, concat_axis=0, tiled=True)
    got_rows = got[:, :, :model_width]
    got_cot = got[:, :, model_width:]

    back, grad_g, grad_u = expert_math(got_rows, got_cot, w_gate[0], w_up[0])

    returned = lax.all_to_all(back, ("expert", "dp"), split_axis=0, concat_axis=0, tiled=True)
    pick_dup = jnp.broadcast_to(
        pick.reshape(n_experts, 1, most_rows, tok_rows), (n_experts, n_dp, most_rows, tok_rows)
    ).reshape(n_experts * n_dp, most_rows, tok_rows)
    grad_tokens = lax.dot_general(
        pick_dup.astype(jnp.float32),
        returned,
        (((0, 1), (0, 1)), ((), ())),
        precision=lax.Precision.HIGHEST,
        preferred_element_type=jnp.float32,
    ).astype(jnp.bfloat16)
    return grad_tokens, grad_g[None], grad_u[None]


def solution(mesh):
    placed = (
        P(("expert", "dp"), None),
        P(("expert", "dp"), None),
        P(("expert", "dp"), None),
        P("expert", None, "dp"),
        P("expert", None, "dp"),
    )
    return jax.shard_map(
        per_device,
        mesh=mesh,
        in_specs=placed,
        out_specs=(P(("expert", "dp"), None), P("expert", None, "dp"), P("expert", None, "dp")),
        check_vma=False,
    )
```

```python
import jax
import jax.numpy as jnp
from jax import lax
from jax.sharding import PartitionSpec as P


def expert_math(rows, cot, weight_gate, weight_up):
    half_width = weight_gate.shape[1]
    both_act = jnp.einsum(
        "skd,df->skf",
        rows,
        jnp.concatenate([weight_gate, weight_up], axis=1),
        preferred_element_type=jnp.float32,
    )
    gate_act = both_act[:, :, :half_width]
    up_act = both_act[:, :, half_width:]
    sigmoid_gate = jax.nn.sigmoid(gate_act)
    cot_float = cot.astype(jnp.float32)
    d_up = (cot_float * gate_act * sigmoid_gate).astype(jnp.bfloat16)
    d_gate = (
        cot_float * up_act * sigmoid_gate * (1.0 + gate_act * (1.0 - sigmoid_gate))
    ).astype(jnp.bfloat16)
    back = jnp.einsum(
        "skf,df->skd",
        jnp.concatenate([d_gate, d_up], axis=2),
        jnp.concatenate([weight_gate, weight_up], axis=1),
        preferred_element_type=jnp.float32,
    )
    grad_g = jnp.einsum("skd,skf->df", rows, d_gate, preferred_element_type=jnp.float32)
    grad_u = jnp.einsum("skd,skf->df", rows, d_up, preferred_element_type=jnp.float32)
    return back.astype(jnp.bfloat16), grad_g.astype(jnp.bfloat16), grad_u.astype(jnp.bfloat16)


def per_device(tokens, cotangent, routing, w_gate, w_up):
    n_experts = lax.axis_size("expert")
    n_dp = lax.axis_size("dp")
    tok_rows, model_width = tokens.shape
    hidden = cotangent.shape[1]
    half_width = hidden // n_dp
    most_rows = max(2, tok_rows // 32, tok_rows // n_experts)
    slot_total = n_experts * most_rows

    expert_of = routing[:, 0]
    one_hot = (expert_of[:, None] == jnp.arange(n_experts, dtype=jnp.int32)[None, :]).astype(
        jnp.int32
    )
    slot_of = jnp.sum(jnp.cumsum(one_hot, axis=0) * one_hot, axis=1) - 1
    dest = expert_of * most_rows + slot_of
    pick = (jnp.arange(slot_total, dtype=jnp.int32)[:, None] == dest[None, :]).astype(
        jnp.bfloat16
    )
    send_rows = jnp.dot(pick, tokens, preferred_element_type=jnp.float32).astype(jnp.bfloat16)
    send_cot = jnp.dot(pick, cotangent, preferred_element_type=jnp.float32).astype(jnp.bfloat16)
    send_rows = send_rows.reshape(n_experts, 1, most_rows, model_width)
    send_cot = jnp.swapaxes(
        send_cot.reshape(n_experts, most_rows, n_dp, half_width), 1, 2
    )
    packed = jnp.concatenate(
        [
            jnp.broadcast_to(send_rows, (n_experts, n_dp, most_rows, model_width)),
            send_cot,
        ],
        axis=3,
    ).reshape(n_experts * n_dp * most_rows, model_width + half_width)
    packed = packed.reshape(n_experts * n_dp, most_rows, model_width + half_width)
    got = lax.all_to_all(packed, ("expert", "dp"), split_axis=0, concat_axis=0, tiled=True)
    got_rows = got[:, :, :model_width]
    got_cot = got[:, :, model_width:]

    back, grad_g, grad_u = expert_math(got_rows, got_cot, w_gate[0], w_up[0])

    returned = lax.all_to_all(back, ("expert", "dp"), split_axis=0, concat_axis=0, tiled=True)
    pick_dup = jnp.broadcast_to(
        pick.reshape(n_experts, 1, most_rows, tok_rows), (n_experts, n_dp, most_rows, tok_rows)
    ).reshape(n_experts * n_dp, most_rows, tok_rows)
    grad_tokens = lax.dot_general(
        pick_dup, returned, (((0, 1), (0, 1)), ((), ())), preferred_element_type=jnp.float32
    ).astype(jnp.bfloat16)
    return grad_tokens, grad_g[None], grad_u[None]


def solution(mesh):
    placed = (
        P(("expert", "dp"), None),
        P(("expert", "dp"), None),
        P(("expert", "dp"), None),
        P("expert", None, "dp"),
        P("expert", None, "dp"),
    )
    return jax.shard_map(
        per_device,
        mesh=mesh,
        in_specs=placed,
        out_specs=(P(("expert", "dp"), None), P("expert", None, "dp"), P("expert", None, "dp")),
        check_vma=False,
    )
```

```python
import jax
import jax.numpy as jnp
from jax import lax
from jax.sharding import PartitionSpec as P


def expert_math(rows, cot, weight_gate, weight_up):
    gate_act = jnp.einsum("skd,df->skf", rows, weight_gate, preferred_element_type=jnp.float32)
    up_act = jnp.einsum("skd,df->skf", rows, weight_up, preferred_element_type=jnp.float32)
    sigmoid_gate = jax.nn.sigmoid(gate_act)
    cot_float = cot.astype(jnp.float32)
    d_up = (cot_float * gate_act * sigmoid_gate).astype(jnp.bfloat16)
    d_gate = (
        cot_float * up_act * sigmoid_gate * (1.0 + gate_act * (1.0 - sigmoid_gate))
    ).astype(jnp.bfloat16)
    back = jnp.einsum(
        "skf,df->skd",
        jnp.concatenate([d_gate, d_up], axis=2),
        jnp.concatenate([weight_gate, weight_up], axis=1),
        preferred_element_type=jnp.float32,
    )
    grad_g = jnp.einsum("skd,skf->df", rows, d_gate, preferred_element_type=jnp.float32)
    grad_u = jnp.einsum("skd,skf->df", rows, d_up, preferred_element_type=jnp.float32)
    return back.astype(jnp.bfloat16), grad_g.astype(jnp.bfloat16), grad_u.astype(jnp.bfloat16)


def per_device(tokens, cotangent, routing, w_gate, w_up):
    n_experts = lax.axis_size("expert")
    n_dp = lax.axis_size("dp")
    tok_rows, model_width = tokens.shape
    hidden = cotangent.shape[1]
    half_width = hidden // n_dp
    most_rows = max(2, tok_rows // 32, tok_rows // n_experts)
    slot_total = n_experts * most_rows

    expert_of = routing[:, 0]
    same = expert_of[:, None] == expert_of[None, :]
    earlier = jnp.arange(tok_rows, dtype=jnp.int32)[None, :] < jnp.arange(
        tok_rows, dtype=jnp.int32
    )[:, None]
    slot_of = jnp.sum((same & earlier).astype(jnp.int32), axis=1)
    dest = expert_of * most_rows + slot_of
    pick = (jnp.arange(slot_total, dtype=jnp.int32)[:, None] == dest[None, :]).astype(
        jnp.bfloat16
    )
    send_rows = jnp.dot(pick, tokens, preferred_element_type=jnp.float32).astype(jnp.bfloat16)
    send_cot = jnp.dot(pick, cotangent, preferred_element_type=jnp.float32).astype(jnp.bfloat16)
    send_rows = send_rows.reshape(n_experts, 1, most_rows, model_width)
    send_cot = jnp.swapaxes(
        send_cot.reshape(n_experts, most_rows, n_dp, half_width), 1, 2
    )
    packed = jnp.concatenate(
        [
            jnp.broadcast_to(send_rows, (n_experts, n_dp, most_rows, model_width)),
            send_cot,
        ],
        axis=3,
    ).reshape(n_experts * n_dp * most_rows, model_width + half_width)
    packed = packed.reshape(n_experts * n_dp, most_rows, model_width + half_width)
    got = lax.all_to_all(packed, ("expert", "dp"), split_axis=0, concat_axis=0, tiled=True)
    got_rows = got[:, :, :model_width]
    got_cot = got[:, :, model_width:]

    back, grad_g, grad_u = expert_math(got_rows, got_cot, w_gate[0], w_up[0])

    returned = lax.all_to_all(back, ("expert", "dp"), split_axis=0, concat_axis=0, tiled=True)
    pick_dup = jnp.broadcast_to(
        pick.reshape(n_experts, 1, most_rows, tok_rows), (n_experts, n_dp, most_rows, tok_rows)
    ).reshape(n_experts * n_dp, most_rows, tok_rows)
    grad_tokens = lax.dot_general(
        pick_dup, returned, (((0, 1), (0, 1)), ((), ())), preferred_element_type=jnp.float32
    ).astype(jnp.bfloat16)
    return grad_tokens, grad_g[None], grad_u[None]


def solution(mesh):
    placed = (
        P(("expert", "dp"), None),
        P(("expert", "dp"), None),
        P(("expert", "dp"), None),
        P("expert", None, "dp"),
        P("expert", None, "dp"),
    )
    return jax.shard_map(
        per_device,
        mesh=mesh,
        in_specs=placed,
        out_specs=(P(("expert", "dp"), None), P("expert", None, "dp"), P("expert", None, "dp")),
        check_vma=False,
    )
```

```python
import jax
import jax.numpy as jnp
from jax import lax
from jax.sharding import PartitionSpec as P


def expert_math(rows, cot, weight_gate, weight_up):
    gate_act = jnp.einsum("skd,df->skf", rows, weight_gate, preferred_element_type=jnp.float32)
    up_act = jnp.einsum("skd,df->skf", rows, weight_up, preferred_element_type=jnp.float32)
    sigmoid_gate = jax.nn.sigmoid(gate_act)
    cot_float = cot.astype(jnp.float32)
    d_up = (cot_float * gate_act * sigmoid_gate).astype(jnp.bfloat16)
    d_gate = (
        cot_float * up_act * sigmoid_gate * (1.0 + gate_act * (1.0 - sigmoid_gate))
    ).astype(jnp.bfloat16)
    back = jnp.einsum(
        "skf,df->skd",
        jnp.concatenate([d_gate, d_up], axis=2),
        jnp.concatenate([weight_gate, weight_up], axis=1),
        preferred_element_type=jnp.float32,
    )
    grad_g = jnp.einsum("skd,skf->df", rows, d_gate, preferred_element_type=jnp.float32)
    grad_u = jnp.einsum("skd,skf->df", rows, d_up, preferred_element_type=jnp.float32)
    return back.astype(jnp.bfloat16), grad_g.astype(jnp.bfloat16), grad_u.astype(jnp.bfloat16)


def per_device(tokens, cotangent, routing, w_gate, w_up):
    n_experts = lax.axis_size("expert")
    n_dp = lax.axis_size("dp")
    tok_rows, model_width = tokens.shape
    hidden = cotangent.shape[1]
    half_width = hidden // n_dp
    most_rows = max(2, tok_rows // 32, tok_rows // n_experts)
    slot_total = n_experts * most_rows

    expert_of = routing[:, 0]
    same = expert_of[:, None] == expert_of[None, :]
    earlier = jnp.arange(tok_rows, dtype=jnp.int32)[None, :] < jnp.arange(
        tok_rows, dtype=jnp.int32
    )[:, None]
    slot_of = jnp.sum((same & earlier).astype(jnp.int32), axis=1)
    dest = expert_of * most_rows + slot_of
    pick = (jnp.arange(slot_total, dtype=jnp.int32)[:, None] == dest[None, :]).astype(
        jnp.bfloat16
    )
    send_rows = jnp.dot(pick, tokens, preferred_element_type=jnp.float32).astype(jnp.bfloat16)
    send_cot = jnp.stack(
        [
            jnp.dot(
                pick,
                cotangent[:, copy * half_width : (copy + 1) * half_width],
                preferred_element_type=jnp.float32,
            )
            .astype(jnp.bfloat16)
            .reshape(n_experts, most_rows, half_width)
            for copy in range(n_dp)
        ],
        axis=1,
    )
    send_rows = send_rows.reshape(n_experts, 1, most_rows, model_width)
    packed = jnp.concatenate(
        [
            jnp.broadcast_to(send_rows, (n_experts, n_dp, most_rows, model_width)),
            send_cot,
        ],
        axis=3,
    ).reshape(n_experts * n_dp * most_rows, model_width + half_width)
    packed = packed.reshape(n_experts * n_dp, most_rows, model_width + half_width)
    got = lax.all_to_all(packed, ("expert", "dp"), split_axis=0, concat_axis=0, tiled=True)
    got_rows = got[:, :, :model_width]
    got_cot = got[:, :, model_width:]

    back, grad_g, grad_u = expert_math(got_rows, got_cot, w_gate[0], w_up[0])

    returned = lax.all_to_all(back, ("expert", "dp"), split_axis=0, concat_axis=0, tiled=True)
    pick_dup = jnp.broadcast_to(
        pick.reshape(n_experts, 1, most_rows, tok_rows), (n_experts, n_dp, most_rows, tok_rows)
    ).reshape(n_experts * n_dp, most_rows, tok_rows)
    grad_tokens = lax.dot_general(
        pick_dup, returned, (((0, 1), (0, 1)), ((), ())), preferred_element_type=jnp.float32
    ).astype(jnp.bfloat16)
    return grad_tokens, grad_g[None], grad_u[None]


def solution(mesh):
    placed = (
        P(("expert", "dp"), None),
        P(("expert", "dp"), None),
        P(("expert", "dp"), None),
        P("expert", None, "dp"),
        P("expert", None, "dp"),
    )
    return jax.shard_map(
        per_device,
        mesh=mesh,
        in_specs=placed,
        out_specs=(P(("expert", "dp"), None), P("expert", None, "dp"), P("expert", None, "dp")),
        check_vma=False,
    )
```

```python
import jax
import jax.numpy as jnp
from jax import lax
from jax.sharding import PartitionSpec as P


def expert_math(rows, cot, weight_gate, weight_up):
    gate_act = jnp.einsum("skd,df->skf", rows, weight_gate, preferred_element_type=jnp.float32)
    up_act = jnp.einsum("skd,df->skf", rows, weight_up, preferred_element_type=jnp.float32)
    sigmoid_gate = jax.nn.sigmoid(gate_act)
    cot_float = cot.astype(jnp.float32)
    d_up = (cot_float * gate_act * sigmoid_gate).astype(jnp.bfloat16)
    d_gate = (
        cot_float * up_act * sigmoid_gate * (1.0 + gate_act * (1.0 - sigmoid_gate))
    ).astype(jnp.bfloat16)
    back = jnp.einsum(
        "skf,df->skd",
        jnp.concatenate([d_gate, d_up], axis=2),
        jnp.concatenate([weight_gate, weight_up], axis=1),
        preferred_element_type=jnp.float32,
    )
    grad_g = jnp.einsum("skd,skf->df", rows, d_gate, preferred_element_type=jnp.float32)
    grad_u = jnp.einsum("skd,skf->df", rows, d_up, preferred_element_type=jnp.float32)
    return back, grad_g.astype(jnp.bfloat16), grad_u.astype(jnp.bfloat16)


def per_device(tokens, cotangent, routing, w_gate, w_up):
    n_experts = lax.axis_size("expert")
    n_dp = lax.axis_size("dp")
    tok_rows, model_width = tokens.shape
    hidden = cotangent.shape[1]
    half_width = hidden // n_dp
    most_rows = max(2, tok_rows // 32, tok_rows // n_experts)
    slot_total = n_experts * most_rows

    expert_of = routing[:, 0]
    same = expert_of[:, None] == expert_of[None, :]
    earlier = jnp.arange(tok_rows, dtype=jnp.int32)[None, :] < jnp.arange(
        tok_rows, dtype=jnp.int32
    )[:, None]
    slot_of = jnp.sum((same & earlier).astype(jnp.int32), axis=1)
    dest = expert_of * most_rows + slot_of
    pick = (jnp.arange(slot_total, dtype=jnp.int32)[:, None] == dest[None, :]).astype(
        jnp.bfloat16
    )
    send_rows = jnp.dot(pick, tokens, preferred_element_type=jnp.float32).astype(jnp.bfloat16)
    send_cot = jnp.dot(pick, cotangent, preferred_element_type=jnp.float32).astype(jnp.bfloat16)
    send_rows = send_rows.reshape(n_experts, 1, most_rows, model_width)
    send_cot = jnp.swapaxes(
        send_cot.reshape(n_experts, most_rows, n_dp, half_width), 1, 2
    )
    packed = jnp.concatenate(
        [
            jnp.broadcast_to(send_rows, (n_experts, n_dp, most_rows, model_width)),
            send_cot,
        ],
        axis=3,
    ).reshape(n_experts * n_dp * most_rows, model_width + half_width)
    packed = packed.reshape(n_experts * n_dp, most_rows, model_width + half_width)
    got = lax.all_to_all(packed, ("expert", "dp"), split_axis=0, concat_axis=0, tiled=True)
    got_rows = got[:, :, :model_width]
    got_cot = got[:, :, model_width:]

    back, grad_g, grad_u = expert_math(got_rows, got_cot, w_gate[0], w_up[0])

    returned = lax.all_to_all(back, ("expert", "dp"), split_axis=0, concat_axis=0, tiled=True)
    pick_dup = jnp.broadcast_to(
        pick.reshape(n_experts, 1, most_rows, tok_rows), (n_experts, n_dp, most_rows, tok_rows)
    ).reshape(n_experts * n_dp, most_rows, tok_rows)
    grad_tokens = lax.dot_general(
        pick_dup.astype(jnp.float32),
        returned,
        (((0, 1), (0, 1)), ((), ())),
        precision=lax.Precision.HIGHEST,
        preferred_element_type=jnp.float32,
    ).astype(jnp.bfloat16)
    return grad_tokens, grad_g[None], grad_u[None]


def solution(mesh):
    placed = (
        P(("expert", "dp"), None),
        P(("expert", "dp"), None),
        P(("expert", "dp"), None),
        P("expert", None, "dp"),
        P("expert", None, "dp"),
    )
    return jax.shard_map(
        per_device,
        mesh=mesh,
        in_specs=placed,
        out_specs=(P(("expert", "dp"), None), P("expert", None, "dp"), P("expert", None, "dp")),
        check_vma=False,
    )
```

```python
import jax
import jax.numpy as jnp
from jax import lax
from jax.sharding import PartitionSpec as P


def expert_math(rows, cot, weight_gate, weight_up):
    gate_act = jnp.einsum("skd,df->skf", rows, weight_gate, preferred_element_type=jnp.float32)
    up_act = jnp.einsum("skd,df->skf", rows, weight_up, preferred_element_type=jnp.float32)
    sigmoid_gate = jax.nn.sigmoid(gate_act)
    cot_float = cot.astype(jnp.float32)
    d_up = (cot_float * gate_act * sigmoid_gate).astype(jnp.bfloat16)
    d_gate = (
        cot_float * up_act * sigmoid_gate * (1.0 + gate_act * (1.0 - sigmoid_gate))
    ).astype(jnp.bfloat16)
    back = jnp.einsum(
        "skf,df->skd",
        jnp.concatenate([d_gate, d_up], axis=2),
        jnp.concatenate([weight_gate, weight_up], axis=1),
        preferred_element_type=jnp.float32,
    )
    grad_g = jnp.einsum("skd,skf->df", rows, d_gate, preferred_element_type=jnp.float32)
    grad_u = jnp.einsum("skd,skf->df", rows, d_up, preferred_element_type=jnp.float32)
    return back.astype(jnp.bfloat16), grad_g.astype(jnp.bfloat16), grad_u.astype(jnp.bfloat16)


def per_device(tokens, cotangent, routing, w_gate, w_up):
    n_experts = lax.axis_size("expert")
    n_dp = lax.axis_size("dp")
    tok_rows, model_width = tokens.shape
    hidden = cotangent.shape[1]
    half_width = hidden // n_dp
    most_rows = max(2, tok_rows // 32, tok_rows // n_experts)
    slot_total = n_experts * most_rows

    expert_of = routing[:, 0]
    same = expert_of[:, None] == expert_of[None, :]
    earlier = jnp.arange(tok_rows, dtype=jnp.int32)[None, :] < jnp.arange(
        tok_rows, dtype=jnp.int32
    )[:, None]
    slot_of = jnp.sum((same & earlier).astype(jnp.int32), axis=1)
    dest = expert_of * most_rows + slot_of
    pick = (jnp.arange(slot_total, dtype=jnp.int32)[:, None] == dest[None, :]).astype(
        jnp.bfloat16
    )
    send_both = jnp.dot(
        pick, jnp.concatenate([tokens, cotangent], axis=1), preferred_element_type=jnp.float32
    ).astype(jnp.bfloat16)
    send_rows = send_both[:, :model_width]
    send_cot = send_both[:, model_width:]
    send_rows = send_rows.reshape(n_experts, 1, most_rows, model_width)
    send_cot = jnp.swapaxes(
        send_cot.reshape(n_experts, most_rows, n_dp, half_width), 1, 2
    )
    packed = jnp.concatenate(
        [
            jnp.broadcast_to(send_rows, (n_experts, n_dp, most_rows, model_width)),
            send_cot,
        ],
        axis=3,
    ).reshape(n_experts * n_dp * most_rows, model_width + half_width)
    packed = packed.reshape(n_experts * n_dp, most_rows, model_width + half_width)
    got = lax.all_to_all(packed, ("expert", "dp"), split_axis=0, concat_axis=0, tiled=True)
    got_rows = got[:, :, :model_width]
    got_cot = got[:, :, model_width:]

    back, grad_g, grad_u = expert_math(got_rows, got_cot, w_gate[0], w_up[0])

    returned = lax.all_to_all(back, ("expert", "dp"), split_axis=0, concat_axis=0, tiled=True)
    pick_dup = jnp.broadcast_to(
        pick.reshape(n_experts, 1, most_rows, tok_rows), (n_experts, n_dp, most_rows, tok_rows)
    ).reshape(n_experts * n_dp, most_rows, tok_rows)
    grad_tokens = lax.dot_general(
        pick_dup, returned, (((0, 1), (0, 1)), ((), ())), preferred_element_type=jnp.float32
    ).astype(jnp.bfloat16)
    return grad_tokens, grad_g[None], grad_u[None]


def solution(mesh):
    placed = (
        P(("expert", "dp"), None),
        P(("expert", "dp"), None),
        P(("expert", "dp"), None),
        P("expert", None, "dp"),
        P("expert", None, "dp"),
    )
    return jax.shard_map(
        per_device,
        mesh=mesh,
        in_specs=placed,
        out_specs=(P(("expert", "dp"), None), P("expert", None, "dp"), P("expert", None, "dp")),
        check_vma=False,
    )
```

```python
import jax
import jax.numpy as jnp
from jax import lax
from jax.sharding import PartitionSpec as P


def expert_math(rows, cot, weight_gate, weight_up):
    gate_act = jnp.einsum("skd,df->skf", rows, weight_gate, preferred_element_type=jnp.float32)
    up_act = jnp.einsum("skd,df->skf", rows, weight_up, preferred_element_type=jnp.float32)
    sigmoid_gate = jax.nn.sigmoid(gate_act)
    cot_float = cot.astype(jnp.float32)
    d_up = (cot_float * gate_act * sigmoid_gate).astype(jnp.bfloat16)
    d_gate = (
        cot_float * up_act * sigmoid_gate * (1.0 + gate_act * (1.0 - sigmoid_gate))
    ).astype(jnp.bfloat16)
    back = jnp.einsum(
        "skf,df->skd",
        jnp.concatenate([d_gate, d_up], axis=2),
        jnp.concatenate([weight_gate, weight_up], axis=1),
        preferred_element_type=jnp.float32,
    )
    grad_g = jnp.einsum("skd,skf->df", rows, d_gate, preferred_element_type=jnp.float32)
    grad_u = jnp.einsum("skd,skf->df", rows, d_up, preferred_element_type=jnp.float32)
    return back.astype(jnp.bfloat16), grad_g.astype(jnp.bfloat16), grad_u.astype(jnp.bfloat16)


def per_device(tokens, cotangent, routing, w_gate, w_up):
    n_experts = lax.axis_size("expert")
    n_dp = lax.axis_size("dp")
    tok_rows, model_width = tokens.shape
    hidden = cotangent.shape[1]
    half_width = hidden // n_dp
    most_rows = max(2, tok_rows // 32, tok_rows // n_experts)
    slot_total = n_experts * most_rows

    expert_of = routing[:, 0]
    same = expert_of[:, None] == expert_of[None, :]
    earlier = jnp.arange(tok_rows, dtype=jnp.int32)[None, :] < jnp.arange(
        tok_rows, dtype=jnp.int32
    )[:, None]
    slot_of = jnp.sum((same & earlier).astype(jnp.int32), axis=1)
    dest = expert_of * most_rows + slot_of
    pick = (jnp.arange(slot_total, dtype=jnp.int32)[:, None] == dest[None, :]).astype(
        jnp.bfloat16
    )
    send_rows = jnp.dot(pick, tokens, preferred_element_type=jnp.float32).astype(jnp.bfloat16)
    send_cot = jnp.dot(pick, cotangent, preferred_element_type=jnp.float32).astype(jnp.bfloat16)
    send_rows = send_rows.reshape(n_experts, 1, most_rows, model_width)
    send_cot = jnp.swapaxes(
        send_cot.reshape(n_experts, most_rows, n_dp, half_width), 1, 2
    )
    packed = jnp.concatenate(
        [
            jnp.broadcast_to(send_rows, (n_experts, n_dp, most_rows, model_width)),
            send_cot,
        ],
        axis=3,
    ).reshape(n_experts * n_dp * most_rows, model_width + half_width)
    packed = packed.reshape(n_experts * n_dp, most_rows, model_width + half_width)
    got = lax.all_to_all(packed, ("expert", "dp"), split_axis=0, concat_axis=0, tiled=True)
    got_rows = got[:, :, :model_width]
    got_cot = got[:, :, model_width:]

    back, grad_g, grad_u = expert_math(got_rows, got_cot, w_gate[0], w_up[0])

    returned = lax.all_to_all(back, ("expert", "dp"), split_axis=0, concat_axis=0, tiled=True)
    source = jnp.arange(n_experts * n_dp, dtype=jnp.int32)[:, None, None]
    slot = jnp.arange(most_rows, dtype=jnp.int32)[None, :, None]
    pick_dup = ((source // n_dp) * most_rows + slot == dest[None, None, :]).astype(jnp.bfloat16)
    grad_tokens = lax.dot_general(
        pick_dup, returned, (((0, 1), (0, 1)), ((), ())), preferred_element_type=jnp.float32
    ).astype(jnp.bfloat16)
    return grad_tokens, grad_g[None], grad_u[None]


def solution(mesh):
    placed = (
        P(("expert", "dp"), None),
        P(("expert", "dp"), None),
        P(("expert", "dp"), None),
        P("expert", None, "dp"),
        P("expert", None, "dp"),
    )
    return jax.shard_map(
        per_device,
        mesh=mesh,
        in_specs=placed,
        out_specs=(P(("expert", "dp"), None), P("expert", None, "dp"), P("expert", None, "dp")),
        check_vma=False,
    )
```

```python
import jax
import jax.numpy as jnp
from jax import lax
from jax.sharding import PartitionSpec as P


def expert_math(rows, cot, weight_gate, weight_up):
    half_width = weight_gate.shape[1]
    both_act = jnp.einsum(
        "skd,df->skf",
        rows,
        jnp.concatenate([weight_gate, weight_up], axis=1),
        preferred_element_type=jnp.float32,
    )
    gate_act = both_act[:, :, :half_width]
    up_act = both_act[:, :, half_width:]
    sigmoid_gate = jax.nn.sigmoid(gate_act)
    cot_float = cot.astype(jnp.float32)
    d_up = (cot_float * gate_act * sigmoid_gate).astype(jnp.bfloat16)
    d_gate = (
        cot_float * up_act * sigmoid_gate * (1.0 + gate_act * (1.0 - sigmoid_gate))
    ).astype(jnp.bfloat16)
    back = jnp.einsum(
        "skf,df->skd",
        jnp.concatenate([d_gate, d_up], axis=2),
        jnp.concatenate([weight_gate, weight_up], axis=1),
        preferred_element_type=jnp.float32,
    )
    grad_g = jnp.einsum("skd,skf->df", rows, d_gate, preferred_element_type=jnp.float32)
    grad_u = jnp.einsum("skd,skf->df", rows, d_up, preferred_element_type=jnp.float32)
    return back.astype(jnp.bfloat16), grad_g.astype(jnp.bfloat16), grad_u.astype(jnp.bfloat16)


def per_device(tokens, cotangent, routing, w_gate, w_up):
    n_experts = lax.axis_size("expert")
    n_dp = lax.axis_size("dp")
    tok_rows, model_width = tokens.shape
    hidden = cotangent.shape[1]
    half_width = hidden // n_dp
    most_rows = max(2, tok_rows // 32, tok_rows // n_experts)
    slot_total = n_experts * most_rows

    expert_of = routing[:, 0]
    same = expert_of[:, None] == expert_of[None, :]
    earlier = jnp.arange(tok_rows, dtype=jnp.int32)[None, :] < jnp.arange(
        tok_rows, dtype=jnp.int32
    )[:, None]
    slot_of = jnp.sum((same & earlier).astype(jnp.int32), axis=1)
    dest = expert_of * most_rows + slot_of
    pick = (jnp.arange(slot_total, dtype=jnp.int32)[:, None] == dest[None, :]).astype(
        jnp.bfloat16
    )
    send_rows = jnp.dot(pick, tokens, preferred_element_type=jnp.float32).astype(jnp.bfloat16)
    send_cot = jnp.dot(pick, cotangent, preferred_element_type=jnp.float32).astype(jnp.bfloat16)
    send_rows = send_rows.reshape(n_experts, 1, most_rows, model_width)
    send_cot = jnp.swapaxes(
        send_cot.reshape(n_experts, most_rows, n_dp, half_width), 1, 2
    )
    packed = jnp.concatenate(
        [
            jnp.broadcast_to(send_rows, (n_experts, n_dp, most_rows, model_width)),
            send_cot,
        ],
        axis=3,
    ).reshape(n_experts * n_dp * most_rows, model_width + half_width)
    packed = packed.reshape(n_experts * n_dp, most_rows, model_width + half_width)
    got = lax.all_to_all(packed, ("expert", "dp"), split_axis=0, concat_axis=0, tiled=True)
    got_rows = got[:, :, :model_width]
    got_cot = got[:, :, model_width:]

    back, grad_g, grad_u = expert_math(got_rows, got_cot, w_gate[0], w_up[0])

    returned = lax.all_to_all(back, ("expert", "dp"), split_axis=0, concat_axis=0, tiled=True)
    pick_dup = jnp.broadcast_to(
        pick.reshape(n_experts, 1, most_rows, tok_rows), (n_experts, n_dp, most_rows, tok_rows)
    ).reshape(n_experts * n_dp, most_rows, tok_rows)
    grad_tokens = lax.dot_general(
        pick_dup, returned, (((0, 1), (0, 1)), ((), ())), preferred_element_type=jnp.float32
    ).astype(jnp.bfloat16)
    return grad_tokens, grad_g[None], grad_u[None]


def solution(mesh):
    placed = (
        P(("expert", "dp"), None),
        P(("expert", "dp"), None),
        P(("expert", "dp"), None),
        P("expert", None, "dp"),
        P("expert", None, "dp"),
    )
    return jax.shard_map(
        per_device,
        mesh=mesh,
        in_specs=placed,
        out_specs=(P(("expert", "dp"), None), P("expert", None, "dp"), P("expert", None, "dp")),
        check_vma=False,
    )
```
